256 devices in a mesh: seq: 64 (over y, z, core), rep: 4 (over x).
Axes of the slice: x: 4, y: 4, z: 8, core: 2. Of those that a mesh axis runs over, the one named last changes fastest.
Arguments:
- tokens: bfloat16 [64, 4, 2048], P('rep'), may hold values from -6 to 6
- lengths: int32 [64], P('rep'), may hold values from 1 to 8192, as said below
- groups: int32 [64], P('rep'), may hold values from 0 to 3
- cache: bfloat16 [4, 8192, 576], P(None, 'seq'), may hold values from -128 to 128
- attn_gain: float32 [2048], replicated, may hold values from 0.3 to 3
- kv_gain: float32 [512], replicated, may hold values from 0.3 to 3
- w_query: bfloat16 [2048, 3072], P('seq'), may hold values from -0.125 to 0.125
- w_latent: bfloat16 [2048, 576], P('seq'), may hold values from -0.25 to 0.25
- w_expand: bfloat16 [512, 4096], P('seq'), may hold values from -0.25 to 0.25
- w_out: bfloat16 [2048, 2048], P('seq'), may hold values from -0.125 to 0.125
- ffn_gain: float32 [2048], replicated, may hold values from 0.5 to 1.5
- w_router: bfloat16 [2048, 64], replicated, may hold values from -5 to 5
- routes: int32 [64, 4, 6], replicated, may hold values from 0 to 63, all different within a row; in each aligned block of 64 rows (0 to 63, 64 to 127, ..., all dimensions but the last counted through in order) at most 12 rows name the same one
- expert_in: bfloat16 [64, 2, 2048, 1408], P('seq', None, None, 'rep'), may hold values from -0.125 to 0.125
- expert_out: bfloat16 [64, 1408, 2048], P('seq', 'rep'), may hold values from -0.15625 to 0.15625
- shared_in: bfloat16 [2, 2048, 2816], P(None, 'seq', 'rep'), may hold values from -0.125 to 0.125
- shared_out: bfloat16 [2816, 2048], P('rep', 'seq'), may hold values from -0.109375 to 0.109375
Outputs:
- layer_out: bfloat16 [64, 4, 2048], P('rep')
The draws below stay inside these ranges and needn't reach their ends.
Inputs may be any that keep to these rules, and one draw needn't show every extreme that they name: Request b reads cache rows 0 to lengths[b] - 1 of its group; some request reads all 8192 rows. `routes`: in each aligned block of 64 rows (the tokens of one index of rep) no expert is named by more than 12 rows.
All inputs are finite; a program needn't handle non-finite values.
Results may differ from the reference program's by a relative error of at most 0.018.
The reference program's roundings to bfloat16 on the way count: a program that leaves them out, or rounds other values in their place, can miss the bound.
Values may be sent and summed in bfloat16 or wider, within the bound.
No kernel may reach another device: no remote copies, remote signals or barrier semaphores. Data moves between devices by JAX's collectives and lax.ppermute only.
A program may use at most 320 MiB of HBM per device.

```python
import math
import jax
import jax.numpy as jnp
import numpy as np
from jax import lax

D = 2048
H = 16
DN = 128
DR = 64
KVL = 512
FF = 1408
SH = 2816
TOPK = 6
NTOK = 4
PROMPT_GROUPS = 4
EXPERTS = 64
TOKR = 64
REQ = 64
CONTEXT_SLOTS = 8192
CAP = 12
N_REP = 4


def draw_lengths(key, part):
    offset_start = jax.random.randint(jax.random.fold_in(key, 11), (REQ,), 1, CONTEXT_SLOTS + 1)
    marked = jax.random.randint(jax.random.fold_in(key, 12), (), 0, REQ)
    return jnp.where(jnp.arange(REQ) == marked, CONTEXT_SLOTS, offset_start).astype(jnp.int32)


def draw_cache(key, part):
    shape = (PROMPT_GROUPS, CONTEXT_SLOTS, KVL + DR)
    value_rows = jnp.clip(jax.random.normal(jax.random.fold_in(key, 24), shape, jnp.float32), -4.0, 4.0)
    return value_rows.astype(jnp.bfloat16)


def draw_w_router(key, part):
    shape = (D, EXPERTS)
    spread = 4.0 / math.sqrt(D)
    value_rows = jnp.clip(jax.random.normal(jax.random.fold_in(key, 33), shape, jnp.float32), -5.0, 5.0) * spread
    return value_rows.astype(jnp.bfloat16)


def set_ends(result, key, low, top_value):
    shape = result.shape
    spot = [jax.random.randint(jax.random.fold_in(key, axis), (), 0, shape[axis]) for axis in range(len(shape))]
    result = result.at[tuple(spot)].set(low)
    longest = shape.index(max(shape))
    spot[longest] = (spot[longest] + 1) % shape[longest]
    return result.at[tuple(spot)].set(top_value)


def block_scale(key, extent, cuts, least, largest):
    level = 1.0
    for dim, shards_of in cuts:
        steps = jax.random.uniform(jax.random.fold_in(jax.random.fold_in(key, 6), dim), (shards_of,), jnp.float32, least / len(cuts), largest / len(cuts))
        level = level * jnp.repeat(jnp.exp(steps), extent[dim] // shards_of).reshape((-1,) + (1,) * (len(extent) - 1 - dim))
    return level


def assign_block(own_key, own, number, rows, number_of, top, limit, skew):
    ranking = jax.random.permutation(own_key, number_of)
    packed, usual = load_shares(number_of, rows * top, limit, skew, True), load_shares(number_of, rows * top, limit, skew, False)
    places = jnp.arange(number_of)

    def named(sizes, turn):
        used = int((sizes > 0).sum())
        fixed = max(1, used // 4)
        shifted = fixed + (places - fixed + turn * (used - fixed)) % max(1, number_of - fixed)
        return jnp.zeros((number_of,), jnp.int32).at[ranking[jnp.where(places < fixed, places, shifted)]].set(jnp.asarray(sizes, jnp.int32))

    sizes = jnp.where(number % 4 == 0, named(packed, number // 4), named(usual, number - number // 4 - 1))
    mixed = jax.random.permutation(jax.random.fold_in(own, 3), number_of)
    source_of, taker = mixed[0:number_of // 2 * 2:2], mixed[1:number_of // 2 * 2:2]
    slack = jnp.minimum(sizes[source_of] - 1, limit - sizes[taker]) // 2
    slack = jnp.where((source_of == ranking[0]) | (taker == ranking[0]) | (sizes[taker] == 0), 0, jnp.maximum(slack, 0))
    shifted = jax.random.randint(jax.random.fold_in(own, 4), (number_of // 2,), 0, 1 << 20) % (slack + 1)
    sizes = sizes.at[source_of].add(-shifted).at[taker].add(shifted)
    labels = jnp.searchsorted(jnp.cumsum(sizes), jnp.arange(rows * top), side="right").astype(jnp.int32)
    listing = labels.reshape(top, rows).T
    listing = listing[jax.random.permutation(jax.random.fold_in(own, 1), rows)]
    turn = jax.random.randint(jax.random.fold_in(own, 2), (rows, 1), 0, top)
    return jnp.take_along_axis(listing, (jnp.arange(top)[None, :] + turn) % top, axis=1)


def load_shares(count, total, most, slope, full):
    portions = [(1 << 20) // math.isqrt(grade ** slope) + 1 for grade in range(1, count + 1)]
    largest = most if full else min(most, max(-(-total // count), total * portions[0] // sum(portions)))
    least = 1 if total - largest >= count - 1 else 0
    holding, surplus = [largest] + [least] * (count - 1), total - largest - least * (count - 1)
    while surplus > 0:
        movable = [i for i in range(1, count) if holding[i] < largest] or [i for i in range(1, count) if holding[i] < most]
        whole, left = sum([portions[i] for i in movable]), surplus
        for i in movable:
            addition = min(most - holding[i], max(1, left * portions[i] // whole), surplus)
            holding[i] = holding[i] + addition
            surplus = surplus - addition
    return np.array(holding)


def normal_values(rng, dims, scale, most, shards=(), kind=jnp.bfloat16):
    result = jax.random.normal(rng, dims, jnp.float32) * scale
    if len(shards) > 0:
        result = block_scale(rng, dims, shards, -0.22, 0.18) * result
    return jnp.clip(result, min=-most, max=most).astype(kind)


def setup_inputs(seed: int = 0) -> dict:
    streams_of = jax.random.split(jax.random.key(seed), 18)
    tokens = normal_values(streams_of[0], (REQ, NTOK, D), 1.0, 6.0, ((0, 4),))
    lengths = draw_lengths(jax.random.fold_in(streams_of[17], 71), 0)
    groups = set_ends(jax.random.randint(streams_of[2], (REQ,), 0, PROMPT_GROUPS), jax.random.fold_in(streams_of[2], 1), 0, PROMPT_GROUPS - 1).astype(jnp.int32)
    cache = draw_cache(jax.random.fold_in(streams_of[17], 71), 0)
    attn_gain = jnp.clip(jnp.exp(jax.random.uniform(streams_of[4], (D,), jnp.float32, math.log(0.3), math.log(3.0))), 0.3, 3.0)
    kv_gain = jnp.clip(jnp.exp(jax.random.uniform(streams_of[5], (KVL,), jnp.float32, math.log(0.3), math.log(3.0))), 0.3, 3.0)
    w_query = normal_values(streams_of[6], (D, H * (DN + DR)), D ** -0.5, 0.125, ((0, 64),))
    w_latent = normal_values(streams_of[7], (D, KVL + DR), (D // 4) ** -0.5, 0.25, ((0, 64),))
    w_expand = normal_values(streams_of[8], (KVL, H * 2 * DN), KVL ** -0.5, 0.25, ((0, 64),))
    w_out = normal_values(streams_of[9], (H * DN, D), (H * DN) ** -0.5, 0.125, ((0, 64),))
    ffn_gain = jnp.clip(1.0 + 0.1 * jax.random.normal(streams_of[10], (D,), jnp.float32), 0.5, 1.5)
    w_router = draw_w_router(jax.random.fold_in(streams_of[17], 71), 0)
    routes_keys = jax.random.split(jax.random.fold_in(streams_of[12], 1), REQ * NTOK // TOKR)
    routes_turns = jax.random.permutation(jax.random.fold_in(streams_of[12], 3), REQ * NTOK // TOKR)
    routes = jax.vmap(lambda own, number: assign_block(jax.random.fold_in(streams_of[12], 2), own, number, TOKR, EXPERTS, TOPK, CAP, 2))(routes_keys, routes_turns).reshape((REQ, NTOK, TOPK))
    expert_in = normal_values(streams_of[13], (EXPERTS, 2, D, FF), D ** -0.5, 0.125, ((0, 64), (3, 4)))
    expert_out = normal_values(streams_of[14], (EXPERTS, FF, D), FF ** -0.5, 0.15625, ((0, 64), (1, 4)))
    shared_in = normal_values(streams_of[15], (2, D, SH), D ** -0.5, 0.125, ((1, 64), (2, 4)))
    shared_out = normal_values(streams_of[16], (SH, D), SH ** -0.5, 0.109375, ((0, 4), (1, 64)))
    return dict(tokens=tokens, lengths=lengths, groups=groups, cache=cache, attn_gain=attn_gain, kv_gain=kv_gain, w_query=w_query, w_latent=w_latent, w_expand=w_expand, w_out=w_out, ffn_gain=ffn_gain, w_router=w_router, routes=routes, expert_in=expert_in, expert_out=expert_out, shared_in=shared_in, shared_out=shared_out)


EPS = 1e-06
NEG = -1e+30

def rms_scale(value_rows, gain):
    wide = value_rows.astype(jnp.float32)
    return wide * lax.rsqrt(lax.optimization_barrier(jnp.mean(wide * wide, axis=-1, keepdims=True)) + EPS) * gain

def angles(places, half):
    freq = 10000.0 ** (-jnp.arange(half, dtype=jnp.float32) / half)
    return places.astype(jnp.float32)[..., None] * freq

def rotate(value_rows, theta):
    half = value_rows.shape[-1] // 2
    first, second = (value_rows[..., :half], value_rows[..., half:])
    cosine, sine = (jnp.cos(theta), jnp.sin(theta))
    return jnp.concatenate([first * cosine - second * sine, first * sine + second * cosine], axis=-1)

def reference(tokens, lengths, groups, cache, attn_gain, kv_gain, w_query, w_latent, w_expand, w_out, ffn_gain, w_router, routes, expert_in, expert_out, shared_in, shared_out):
    requests = tokens.shape[0]
    all_rows = requests * NTOK
    scale = (DN + DR) ** (-0.5)
    flat = tokens.reshape(all_rows, D)
    normed = rms_scale(flat, attn_gain).astype(jnp.bfloat16)
    query = jnp.dot(normed, w_query, preferred_element_type=jnp.float32).reshape(all_rows, H, DN + DR)
    latent = jnp.dot(normed, w_latent, preferred_element_type=jnp.float32)
    places = lengths[:, None] + jnp.arange(NTOK, dtype=jnp.int32)[None, :]
    theta = angles(places, DR // 2).reshape(all_rows, DR // 2)
    q_nope = query[:, :, :DN].astype(jnp.bfloat16)
    q_rope = rotate(query[:, :, DN:], theta[:, None, :]).astype(jnp.bfloat16)
    c_new = rms_scale(latent[:, :KVL], kv_gain).astype(jnp.bfloat16)
    k_rope = rotate(latent[:, KVL:], theta).astype(jnp.bfloat16)
    expand = w_expand.reshape(KVL, H, 2, DN)
    q_lat = jnp.einsum('rhn,lhn->rhl', q_nope.astype(jnp.float32), expand[:, :, 0, :].astype(jnp.float32)).astype(jnp.bfloat16)
    q_cat = jnp.concatenate([q_lat, q_rope], axis=-1).reshape(requests, NTOK, H, KVL + DR)
    k_new = jnp.concatenate([c_new, k_rope], axis=-1).reshape(requests, NTOK, KVL + DR)
    lat_new = c_new.reshape(requests, NTOK, KVL)
    causal = jnp.arange(NTOK)[:, None] >= jnp.arange(NTOK)[None, :]
    causal_rows = jnp.repeat(causal, H, axis=0)

    def attend(item):
        q_rows, new_keys, new_lat, length, group = item
        keys = lax.dynamic_index_in_dim(cache, group, 0, keepdims=False)
        rows = q_rows.reshape(NTOK * H, KVL + DR)
        live = jnp.arange(CONTEXT_SLOTS, dtype=jnp.int32) < length
        old = jnp.dot(rows, keys.T, preferred_element_type=jnp.float32) * scale
        old = jnp.where(live[None, :], old, NEG)
        fresh = jnp.dot(rows, new_keys.T, preferred_element_type=jnp.float32) * scale
        fresh = jnp.where(causal_rows, fresh, NEG)
        top = jnp.maximum(lax.optimization_barrier(jnp.max(old, axis=1)), lax.optimization_barrier(jnp.max(fresh, axis=1)))
        old_w = jnp.where(live[None, :], jnp.exp(old - top[:, None]), 0.0)
        fresh_w = jnp.where(causal_rows, jnp.exp(fresh - top[:, None]), 0.0)
        mass = lax.optimization_barrier(jnp.sum(old_w, axis=1)) + lax.optimization_barrier(jnp.sum(fresh_w, axis=1))
        summed = jnp.dot(old_w.astype(jnp.bfloat16), keys[:, :KVL], preferred_element_type=jnp.float32)
        summed = summed + jnp.dot(fresh_w.astype(jnp.bfloat16), new_lat, preferred_element_type=jnp.float32)
        return (summed / mass[:, None]).astype(jnp.bfloat16).reshape(NTOK, H, KVL)
    o_lat = lax.map(attend, (q_cat, k_new, lat_new, lengths, groups)).reshape(all_rows, H, KVL)
    value = jnp.einsum('rhl,lhn->rhn', o_lat.astype(jnp.float32), expand[:, :, 1, :].astype(jnp.float32)).astype(jnp.bfloat16).reshape(all_rows, H * DN)
    attn = jnp.dot(value, w_out, preferred_element_type=jnp.float32)
    resid = (flat.astype(jnp.float32) + attn).astype(jnp.bfloat16)
    normed2 = rms_scale(resid, ffn_gain).astype(jnp.bfloat16)
    gates = jax.nn.softmax(jnp.dot(normed2, w_router, preferred_element_type=jnp.float32), axis=-1)
    chosen = routes.reshape(all_rows, TOPK)
    picked = jnp.take_along_axis(gates, chosen, axis=1)
    slots = N_REP * CAP

    def one_expert(total, item):
        index, w_in, w_down = item
        match = chosen == index
        used = jnp.any(match, axis=1)
        coef = lax.optimization_barrier(jnp.sum(jnp.where(match, picked, 0.0), axis=1))
        where_rows = jnp.nonzero(used, size=slots, fill_value=0)[0].astype(jnp.int32)
        live = jnp.arange(slots, dtype=jnp.int32) < jnp.sum(used.astype(jnp.int32))
        rows = normed2[where_rows].astype(jnp.float32)
        both = jnp.einsum('rd,kdf->krf', rows, w_in.astype(jnp.float32))
        act = (jax.nn.silu(both[0]) * both[1]).astype(jnp.bfloat16)
        outputs = jnp.dot(act, w_down, preferred_element_type=jnp.float32)
        weight = jnp.where(live, coef[where_rows], 0.0)
        return (total.at[where_rows].add(weight[:, None] * outputs), None)
    routed, _ = lax.scan(one_expert, jnp.zeros((all_rows, D), jnp.float32), (jnp.arange(EXPERTS, dtype=jnp.int32), expert_in, expert_out))
    shared_both = jnp.einsum('rd,kdf->krf', normed2.astype(jnp.float32), shared_in.astype(jnp.float32))
    shared_act = (jax.nn.silu(shared_both[0]) * shared_both[1]).astype(jnp.bfloat16)
    shared = jnp.dot(shared_act, shared_out, preferred_element_type=jnp.float32)
    total = resid.astype(jnp.float32) + routed + shared
    return total.astype(jnp.bfloat16).reshape(requests, NTOK, D)
```

```python
import jax
import jax.numpy as jnp
from jax import lax
from jax.sharding import PartitionSpec as P

D = 2048
H = 16
DN = 128
DR = 64
KVL = 512
TOPK = 6
NTOK = 4


EPS = 1e-06
NEG = -1e30


def rms_scale(value_rows, gain):
    wide = value_rows.astype(jnp.float32)
    return wide * lax.rsqrt(jnp.mean(wide * wide, axis=-1, keepdims=True) + EPS) * gain


def angles(places, half):
    freq = 10000.0 ** (-jnp.arange(half, dtype=jnp.float32) / half)
    return places.astype(jnp.float32)[..., None] * freq


def rotate(value_rows, theta):
    half = value_rows.shape[-1] // 2
    first, second = (value_rows[..., :half], value_rows[..., half:])
    cosine, sine = (jnp.cos(theta), jnp.sin(theta))
    return jnp.concatenate(
        [first * cosine - second * sine, first * sine + second * cosine], axis=-1
    )


def scatter_rows(x, axis):
    return lax.all_to_all(x, axis, 0, 0, tiled=True)


def sum_to_owner(x, axis, n):
    got = scatter_rows(x, axis)
    return got.reshape((n, got.shape[0] // n) + got.shape[1:]).astype(jnp.float32).sum(0)


def gather_rows(x, axis, n):
    copies = jnp.broadcast_to(x[None], (n,) + x.shape).reshape((n * x.shape[0],) + x.shape[1:])
    return scatter_rows(copies, axis)


def per_device(
    tokens,
    lengths,
    groups,
    cache,
    attn_gain,
    kv_gain,
    w_query,
    w_latent,
    w_expand,
    w_out,
    ffn_gain,
    w_router,
    routes,
    expert_in,
    expert_out,
    shared_in,
    shared_out,
):
    me = lax.axis_index("seq")
    n = lax.axis_size("seq")
    rep_count = lax.axis_size("rep")
    local_req = tokens.shape[0]
    tok_rows = local_req * NTOK
    head_rows = tok_rows * H
    own = tok_rows // n
    scale = (DN + DR) ** (-0.5)
    flat = tokens.reshape(tok_rows, D)
    expand = lax.all_gather(w_expand, "seq", axis=0, tiled=True).reshape(KVL, H, 2, DN)
    shared_full = lax.all_gather(shared_in, "seq", axis=1, tiled=True)

    normed = rms_scale(flat, attn_gain).astype(jnp.bfloat16)
    slab = w_query.shape[0]
    own_cols = lax.dynamic_slice_in_dim(normed, me * slab, slab, 1)
    part = jnp.concatenate(
        [
            jnp.dot(own_cols, w_query, preferred_element_type=jnp.float32),
            jnp.dot(own_cols, w_latent, preferred_element_type=jnp.float32),
        ],
        axis=1,
    )
    mine = sum_to_owner(part, "seq", n)
    qw = H * (DN + DR)
    rows_idx = me * own + jnp.arange(own, dtype=jnp.int32)
    places = lengths[rows_idx // NTOK] + rows_idx % NTOK
    theta = angles(places, DR // 2)
    query = mine[:, :qw].reshape(own, H, DN + DR)
    latent = mine[:, qw:]
    q_nope = query[:, :, :DN].astype(jnp.bfloat16)
    q_rope = rotate(query[:, :, DN:], theta[:, None, :]).astype(jnp.bfloat16)
    c_new = rms_scale(latent[:, :KVL], kv_gain).astype(jnp.bfloat16)
    k_rope = rotate(latent[:, KVL:], theta).astype(jnp.bfloat16)
    pack = jnp.concatenate(
        [q_nope.reshape(own, H * DN), q_rope.reshape(own, H * DR), c_new, k_rope], axis=1
    )
    every_pack = gather_rows(pack, "seq", n)
    q_nope_all = every_pack[:, : H * DN].reshape(tok_rows, H, DN)
    q_rope_all = every_pack[:, H * DN : H * (DN + DR)].reshape(tok_rows, H, DR)
    k_new_all = every_pack[:, H * (DN + DR) :]
    q_lat = jnp.einsum(
        "rhn,lhn->rhl", q_nope_all, expand[:, :, 0, :], preferred_element_type=jnp.float32
    ).astype(jnp.bfloat16)
    q_cat = jnp.concatenate([q_lat, q_rope_all], axis=-1)
    q_rows = q_cat.reshape(head_rows, KVL + DR)

    row_len = jnp.repeat(lengths, NTOK * H)
    row_grp = jnp.repeat(groups, NTOK * H)
    span = cache.shape[1]
    places_here = me * span + jnp.arange(span, dtype=jnp.int32)
    live = places_here[None, :] < row_len[:, None]
    best = jnp.full((head_rows,), NEG, jnp.float32)
    mass = jnp.zeros((head_rows,), jnp.float32)
    acc = jnp.zeros((head_rows, KVL), jnp.float32)
    for group in range(cache.shape[0]):
        keys = cache[group]
        score = jnp.einsum("rc,jc->rj", q_rows, keys, preferred_element_type=jnp.float32) * scale
        hit = row_grp == group
        valid = live & hit[:, None]
        peak = jnp.max(jnp.where(valid, score, NEG), axis=1)
        expo = jnp.where(valid, jnp.exp(score - peak[:, None]), 0.0)
        summed = jnp.dot(
            expo.astype(jnp.bfloat16), keys[:, :KVL], preferred_element_type=jnp.float32
        )
        best = jnp.where(hit, peak, best)
        mass = jnp.where(hit, jnp.sum(expo, axis=1), mass)
        acc = jnp.where(hit[:, None], summed, acc)

    stats = jnp.concatenate([acc, best[:, None], mass[:, None]], axis=1)
    got = scatter_rows(stats, "seq").reshape(n, own * H, KVL + 2)
    peaks = got[:, :, KVL]
    masses = got[:, :, KVL + 1]
    cached_top = jnp.max(peaks, axis=0)
    q_own = lax.dynamic_slice_in_dim(q_cat, me * own, own, 0)
    k_req = k_new_all.reshape(local_req, NTOK, KVL + DR)[rows_idx // NTOK]
    fresh = jnp.einsum("khc,kuc->khu", q_own, k_req, preferred_element_type=jnp.float32) * scale
    causal = (jnp.arange(NTOK)[None, :] <= (rows_idx % NTOK)[:, None])[:, None, :]
    fresh = jnp.where(causal, fresh, NEG).reshape(own * H, NTOK)
    causal_rows = jnp.broadcast_to(causal, (own, H, NTOK)).reshape(own * H, NTOK)
    top = jnp.maximum(cached_top, jnp.max(fresh, axis=1))
    keep = jnp.exp(peaks - top[None, :])
    fresh_w = jnp.where(causal_rows, jnp.exp(fresh - top[:, None]), 0.0)
    total_mass = jnp.sum(masses * keep, axis=0) + jnp.sum(fresh_w, axis=1)
    fresh_sum = jnp.einsum(
        "khu,kul->khl",
        fresh_w.astype(jnp.bfloat16).reshape(own, H, NTOK),
        k_req[:, :, :KVL],
        preferred_element_type=jnp.float32,
    ).reshape(own * H, KVL)
    total_acc = jnp.sum(got[:, :, :KVL] * keep[:, :, None], axis=0) + fresh_sum
    o_lat = (total_acc / total_mass[:, None]).astype(jnp.bfloat16).reshape(own, H, KVL)
    value = (
        jnp.einsum("khl,lhn->khn", o_lat, expand[:, :, 1, :], preferred_element_type=jnp.float32)
        .astype(jnp.bfloat16)
        .reshape(own, H * DN)
    )

    out_rows = w_out.shape[0]
    cols = value.reshape(own, n, out_rows).transpose(1, 0, 2).reshape(n * own, out_rows)
    value_cols = scatter_rows(cols, "seq")
    attn_part = jnp.dot(value_cols, w_out, preferred_element_type=jnp.float32)
    attn = sum_to_owner(attn_part, "seq", n)
    flat_own = lax.dynamic_slice_in_dim(flat, me * own, own, 0)
    resid_own = (flat_own.astype(jnp.float32) + attn).astype(jnp.bfloat16)
    normed2_own = rms_scale(resid_own, ffn_gain).astype(jnp.bfloat16)
    normed2 = gather_rows(normed2_own, "seq", n)

    every = lax.all_gather(normed2, "rep", axis=0, tiled=True)
    all_rows = every.shape[0]
    gates = jax.nn.softmax(jnp.dot(every, w_router, preferred_element_type=jnp.float32), axis=-1)
    chosen = routes.reshape(all_rows, TOPK)
    picked = jnp.take_along_axis(gates, chosen, axis=1)
    local_exp = expert_in.shape[0]
    own_expert = me * local_exp
    match = chosen == own_expert
    used = jnp.any(match, axis=1)
    coef = jnp.sum(jnp.where(match, picked, 0.0), axis=1)
    cap = max(2, min(tok_rows, 2 * tok_rows * TOPK // (local_exp * n)))
    slots = rep_count * cap
    rank = jnp.cumsum(used.reshape(rep_count, tok_rows).astype(jnp.int32), axis=1) - 1
    slot_of = (jnp.arange(rep_count, dtype=jnp.int32)[:, None] * cap + rank).reshape(all_rows)
    slot_of = jnp.where(used, slot_of, -1)
    pick = jnp.arange(slots, dtype=jnp.int32)[:, None] == slot_of[None, :]
    gathered = jnp.dot(pick.astype(jnp.bfloat16), every, preferred_element_type=jnp.float32).astype(
        jnp.bfloat16
    )
    both = jnp.einsum("rd,kdf->krf", gathered, expert_in[0], preferred_element_type=jnp.float32)
    act = (jax.nn.silu(both[0]) * both[1]).astype(jnp.bfloat16)
    expert_y = jnp.dot(act, expert_out[0], preferred_element_type=jnp.float32)
    shared_both = jnp.einsum(
        "rd,kdf->krf", every, shared_full, preferred_element_type=jnp.float32
    )
    shared_act = (jax.nn.silu(shared_both[0]) * shared_both[1]).astype(jnp.bfloat16)
    shared_part = jnp.dot(shared_act, shared_out, preferred_element_type=jnp.float32)
    out_cols = shared_out.shape[1]
    pick_wide = pick.astype(jnp.float32)
    routed = lax.dot_general(
        pick_wide, expert_y, (((0,), (0,)), ((), ())), precision=lax.Precision.HIGHEST
    )
    routed = routed * coef[:, None]
    block = lax.dynamic_slice_in_dim(routed, me * out_cols, out_cols, 1) + shared_part
    mine_rows = lax.psum_scatter(
        lax.dynamic_update_slice_in_dim(routed, block, me * out_cols, 1).astype(jnp.bfloat16),
        "rep",
        scatter_dimension=0,
        tiled=True,
    )
    total = sum_to_owner(mine_rows, "seq", n)
    out_own = (resid_own.astype(jnp.float32) + total).astype(jnp.bfloat16)
    return gather_rows(out_own, "seq", n).reshape(tokens.shape)


def solution(mesh):
    placed = (
        P("rep", None, None),
        P("rep"),
        P("rep"),
        P(None, "seq", None),
        P(),
        P(),
        P("seq", None),
        P("seq", None),
        P("seq", None),
        P("seq", None),
        P(),
        P(),
        P(),
        P("seq", None, None, "rep"),
        P("seq", "rep", None),
        P(None, "seq", "rep"),
        P("rep", "seq"),
    )
    return jax.shard_map(
        per_device, mesh=mesh, in_specs=placed, out_specs=P("rep", None, None), check_vma=False
    )
```

```python
import jax
import jax.numpy as jnp
from jax import lax
from jax.sharding import PartitionSpec as P

D = 2048
H = 16
DN = 128
DR = 64
KVL = 512
TOPK = 6
NTOK = 4


EPS = 1e-06
NEG = -1e30


def rms_scale(value_rows, gain):
    wide = value_rows.astype(jnp.float32)
    return wide * lax.rsqrt(jnp.mean(wide * wide, axis=-1, keepdims=True) + EPS) * gain


def angles(places, half):
    freq = 10000.0 ** (-jnp.arange(half, dtype=jnp.float32) / half)
    return places.astype(jnp.float32)[..., None] * freq


def rotate(value_rows, theta):
    half = value_rows.shape[-1] // 2
    first, second = (value_rows[..., :half], value_rows[..., half:])
    cosine, sine = (jnp.cos(theta), jnp.sin(theta))
    return jnp.concatenate(
        [first * cosine - second * sine, first * sine + second * cosine], axis=-1
    )


def scatter_rows(x, axis):
    return lax.all_to_all(x, axis, 0, 0, tiled=True)


def sum_to_owner(x, axis, n):
    got = scatter_rows(x, axis)
    return got.reshape((n, got.shape[0] // n) + got.shape[1:]).astype(jnp.float32).sum(0)


def gather_rows(x, axis, n):
    copies = jnp.broadcast_to(x[None], (n,) + x.shape).reshape((n * x.shape[0],) + x.shape[1:])
    return scatter_rows(copies, axis)


def per_device(
    tokens,
    lengths,
    groups,
    cache,
    attn_gain,
    kv_gain,
    w_query,
    w_latent,
    w_expand,
    w_out,
    ffn_gain,
    w_router,
    routes,
    expert_in,
    expert_out,
    shared_in,
    shared_out,
):
    me = lax.axis_index("seq")
    n = lax.axis_size("seq")
    rep_count = lax.axis_size("rep")
    local_req = tokens.shape[0]
    tok_rows = local_req * NTOK
    head_rows = tok_rows * H
    own = tok_rows // n
    scale = (DN + DR) ** (-0.5)
    flat = tokens.reshape(tok_rows, D)
    expand = lax.all_gather(w_expand, "seq", axis=0, tiled=True).reshape(KVL, H, 2, DN)
    shared_full = lax.all_gather(shared_in, "seq", axis=1, tiled=True)

    normed = rms_scale(flat, attn_gain).astype(jnp.bfloat16)
    slab = w_query.shape[0]
    own_cols = lax.dynamic_slice_in_dim(normed, me * slab, slab, 1)
    part = jnp.concatenate(
        [
            jnp.dot(own_cols, w_query, preferred_element_type=jnp.float32),
            jnp.dot(own_cols, w_latent, preferred_element_type=jnp.float32),
        ],
        axis=1,
    )
    mine = sum_to_owner(part, "seq", n)
    qw = H * (DN + DR)
    rows_idx = me * own + jnp.arange(own, dtype=jnp.int32)
    places = lengths[rows_idx // NTOK] + rows_idx % NTOK
    theta = angles(places, DR // 2)
    query = mine[:, :qw].reshape(own, H, DN + DR)
    latent = mine[:, qw:]
    q_nope = query[:, :, :DN].astype(jnp.bfloat16)
    q_rope = rotate(query[:, :, DN:], theta[:, None, :]).astype(jnp.bfloat16)
    c_new = rms_scale(latent[:, :KVL], kv_gain).astype(jnp.bfloat16)
    k_rope = rotate(latent[:, KVL:], theta).astype(jnp.bfloat16)
    pack = jnp.concatenate(
        [q_nope.reshape(own, H * DN), q_rope.reshape(own, H * DR), c_new, k_rope], axis=1
    )
    every_pack = gather_rows(pack, "seq", n)
    q_nope_all = every_pack[:, : H * DN].reshape(tok_rows, H, DN)
    q_rope_all = every_pack[:, H * DN : H * (DN + DR)].reshape(tok_rows, H, DR)
    k_new_all = every_pack[:, H * (DN + DR) :]
    q_lat = jnp.einsum(
        "rhn,lhn->rhl", q_nope_all, expand[:, :, 0, :], preferred_element_type=jnp.float32
    ).astype(jnp.bfloat16)
    q_cat = jnp.concatenate([q_lat, q_rope_all], axis=-1)
    q_rows = q_cat.reshape(head_rows, KVL + DR)

    row_len = jnp.repeat(lengths, NTOK * H)
    row_grp = jnp.repeat(groups, NTOK * H)
    span = cache.shape[1]
    places_here = me * span + jnp.arange(span, dtype=jnp.int32)
    live = places_here[None, :] < row_len[:, None]
    best = jnp.full((head_rows,), NEG, jnp.float32)
    mass = jnp.zeros((head_rows,), jnp.float32)
    acc = jnp.zeros((head_rows, KVL), jnp.float32)
    for group in range(cache.shape[0]):
        keys = cache[group]
        score = jnp.einsum("rc,jc->rj", q_rows, keys, preferred_element_type=jnp.float32) * scale
        hit = row_grp == group
        valid = live & hit[:, None]
        peak = jnp.max(jnp.where(valid, score, NEG), axis=1)
        expo = jnp.where(valid, jnp.exp(score - peak[:, None]), 0.0)
        summed = jnp.dot(
            expo.astype(jnp.bfloat16), keys[:, :KVL], preferred_element_type=jnp.float32
        )
        best = jnp.where(hit, peak, best)
        mass = jnp.where(hit, jnp.sum(expo, axis=1), mass)
        acc = jnp.where(hit[:, None], summed, acc)

    w_v = expand[:, :, 1, :]
    part_v = jnp.einsum(
        "thl,lhn->thn",
        acc.reshape(tok_rows, H, KVL),
        w_v.astype(jnp.float32),
        precision=lax.Precision.HIGHEST,
        preferred_element_type=jnp.float32,
    )
    out_rows = w_out.shape[0]
    per_head = DN // out_rows
    v_cols = part_v.reshape(tok_rows, n, out_rows).transpose(1, 0, 2)
    head_of = jnp.arange(n, dtype=jnp.int32) // per_head
    peak_to = best.reshape(tok_rows, H).T[head_of]
    mass_to = mass.reshape(tok_rows, H).T[head_of]
    send = jnp.concatenate([v_cols, peak_to[..., None], mass_to[..., None]], axis=-1)
    got = scatter_rows(send.reshape(n * tok_rows, out_rows + 2), "seq").reshape(
        n, tok_rows, out_rows + 2
    )
    peaks = got[:, :, out_rows]
    masses = got[:, :, out_rows + 1]
    my_head = me // per_head
    unit0 = (me % per_head) * out_rows
    q_head = lax.dynamic_index_in_dim(q_cat, my_head, 1, keepdims=False)
    fresh = jnp.dot(q_head, k_new_all.T, preferred_element_type=jnp.float32) * scale
    tok = jnp.arange(tok_rows, dtype=jnp.int32)
    causal = ((tok[None, :] // NTOK) == (tok[:, None] // NTOK)) & (tok[None, :] <= tok[:, None])
    fresh = jnp.where(causal, fresh, NEG)
    top = jnp.maximum(jnp.max(peaks, axis=0), jnp.max(fresh, axis=1))
    keep = jnp.exp(peaks - top[None, :])
    fresh_w = jnp.where(causal, jnp.exp(fresh - top[:, None]), 0.0)
    total_mass = jnp.sum(masses * keep, axis=0) + jnp.sum(fresh_w, axis=1)
    fresh_lat = jnp.dot(
        fresh_w.astype(jnp.bfloat16), k_new_all[:, :KVL], preferred_element_type=jnp.float32
    )
    w_v_mine = lax.dynamic_slice_in_dim(
        lax.dynamic_index_in_dim(w_v, my_head, 1, keepdims=False), unit0, out_rows, 1
    )
    fresh_v = jnp.dot(
        fresh_lat,
        w_v_mine.astype(jnp.float32),
        precision=lax.Precision.HIGHEST,
        preferred_element_type=jnp.float32,
    )
    total_v = jnp.sum(got[:, :, :out_rows] * keep[:, :, None], axis=0) + fresh_v
    value_cols = (total_v / total_mass[:, None]).astype(jnp.bfloat16)

    attn_part = jnp.dot(value_cols, w_out, preferred_element_type=jnp.float32)
    attn = sum_to_owner(attn_part, "seq", n)
    flat_own = lax.dynamic_slice_in_dim(flat, me * own, own, 0)
    resid_own = (flat_own.astype(jnp.float32) + attn).astype(jnp.bfloat16)
    normed2_own = rms_scale(resid_own, ffn_gain).astype(jnp.bfloat16)
    normed2 = gather_rows(normed2_own, "seq", n)

    normed2, shared_full = lax.optimization_barrier((normed2, shared_full))
    every = lax.all_gather(normed2, "rep", axis=0, tiled=True)
    all_rows = every.shape[0]
    gates = jax.nn.softmax(jnp.dot(every, w_router, preferred_element_type=jnp.float32), axis=-1)
    chosen = routes.reshape(all_rows, TOPK)
    local_exp = expert_in.shape[0]
    own_expert = me * local_exp
    match = chosen == own_expert
    used = jnp.any(match, axis=1)
    gate_col = lax.dynamic_index_in_dim(gates, own_expert, 1, keepdims=False)
    coef = jnp.where(used, gate_col, 0.0)
    cap = max(2, min(tok_rows, 2 * tok_rows * TOPK // (local_exp * n)))
    slots = rep_count * cap
    rank = jnp.cumsum(used.reshape(rep_count, tok_rows).astype(jnp.int32), axis=1) - 1
    slot_of = (jnp.arange(rep_count, dtype=jnp.int32)[:, None] * cap + rank).reshape(all_rows)
    slot_of = jnp.where(used, slot_of, -1)
    pick = jnp.arange(slots, dtype=jnp.int32)[:, None] == slot_of[None, :]
    gathered = jnp.dot(pick.astype(jnp.bfloat16), every, preferred_element_type=jnp.float32).astype(
        jnp.bfloat16
    )
    both = jnp.einsum("rd,kdf->krf", gathered, expert_in[0], preferred_element_type=jnp.float32)
    act = (jax.nn.silu(both[0]) * both[1]).astype(jnp.bfloat16)
    expert_y = jnp.dot(act, expert_out[0], preferred_element_type=jnp.float32)
    shared_both = jnp.einsum(
        "rd,kdf->krf", every, shared_full, preferred_element_type=jnp.float32
    )
    shared_act = (jax.nn.silu(shared_both[0]) * shared_both[1]).astype(jnp.bfloat16)
    shared_part = jnp.dot(shared_act, shared_out, preferred_element_type=jnp.float32)
    out_cols = shared_out.shape[1]
    pick_wide = pick.astype(jnp.float32)
    routed = lax.dot_general(
        pick_wide, expert_y, (((0,), (0,)), ((), ())), precision=lax.Precision.HIGHEST
    )
    routed = routed * coef[:, None]
    block = lax.dynamic_slice_in_dim(routed, me * out_cols, out_cols, 1) + shared_part
    mine_rows = lax.psum_scatter(
        lax.dynamic_update_slice_in_dim(routed, block, me * out_cols, 1).astype(jnp.bfloat16),
        "rep",
        scatter_dimension=0,
        tiled=True,
    )
    total = sum_to_owner(mine_rows, "seq", n)
    out_own = (resid_own.astype(jnp.float32) + total).astype(jnp.bfloat16)
    return gather_rows(out_own, "seq", n).reshape(tokens.shape)


def solution(mesh):
    placed = (
        P("rep", None, None),
        P("rep"),
        P("rep"),
        P(None, "seq", None),
        P(),
        P(),
        P("seq", None),
        P("seq", None),
        P("seq", None),
        P("seq", None),
        P(),
        P(),
        P(),
        P("seq", None, None, "rep"),
        P("seq", "rep", None),
        P(None, "seq", "rep"),
        P("rep", "seq"),
    )
    return jax.shard_map(
        per_device, mesh=mesh, in_specs=placed, out_specs=P("rep", None, None), check_vma=False
    )
```

```python
import jax
import jax.numpy as jnp
from jax import lax
from jax.sharding import PartitionSpec as P

D = 2048
H = 16
DN = 128
DR = 64
KVL = 512
TOPK = 6
NTOK = 4


EPS = 1e-06
NEG = -1e30


def rms_scale(value_rows, gain):
    wide = value_rows.astype(jnp.float32)
    return wide * lax.rsqrt(jnp.mean(wide * wide, axis=-1, keepdims=True) + EPS) * gain


def angles(places, half):
    freq = 10000.0 ** (-jnp.arange(half, dtype=jnp.float32) / half)
    return places.astype(jnp.float32)[..., None] * freq


def rotate(value_rows, theta):
    half = value_rows.shape[-1] // 2
    first, second = (value_rows[..., :half], value_rows[..., half:])
    cosine, sine = (jnp.cos(theta), jnp.sin(theta))
    return jnp.concatenate(
        [first * cosine - second * sine, first * sine + second * cosine], axis=-1
    )


def scatter_rows(x, axis):
    return lax.all_to_all(x, axis, 0, 0, tiled=True)


def sum_to_owner(x, axis, n):
    got = scatter_rows(x, axis)
    return got.reshape((n, got.shape[0] // n) + got.shape[1:]).astype(jnp.float32).sum(0)


def gather_rows(x, axis, n):
    copies = jnp.broadcast_to(x[None], (n,) + x.shape).reshape((n * x.shape[0],) + x.shape[1:])
    return scatter_rows(copies, axis)


def per_device(
    tokens,
    lengths,
    groups,
    cache,
    attn_gain,
    kv_gain,
    w_query,
    w_latent,
    w_expand,
    w_out,
    ffn_gain,
    w_router,
    routes,
    expert_in,
    expert_out,
    shared_in,
    shared_out,
):
    me = lax.axis_index("seq")
    n = lax.axis_size("seq")
    rep_count = lax.axis_size("rep")
    local_req = tokens.shape[0]
    tok_rows = local_req * NTOK
    head_rows = tok_rows * H
    own = tok_rows // n
    scale = (DN + DR) ** (-0.5)
    flat = tokens.reshape(tok_rows, D)
    expand = lax.all_gather(w_expand, "seq", axis=0, tiled=True).reshape(KVL, H, 2, DN)
    shared_full = lax.all_gather(shared_in, "seq", axis=1, tiled=True)

    normed = rms_scale(flat, attn_gain).astype(jnp.bfloat16)
    slab = w_query.shape[0]
    own_cols = lax.dynamic_slice_in_dim(normed, me * slab, slab, 1)
    part = jnp.concatenate(
        [
            jnp.dot(own_cols, w_query, preferred_element_type=jnp.float32),
            jnp.dot(own_cols, w_latent, preferred_element_type=jnp.float32),
        ],
        axis=1,
    )
    mine = sum_to_owner(part, "seq", n)
    qw = H * (DN + DR)
    rows_idx = me * own + jnp.arange(own, dtype=jnp.int32)
    places = lengths[rows_idx // NTOK] + rows_idx % NTOK
    theta = angles(places, DR // 2)
    query = mine[:, :qw].reshape(own, H, DN + DR)
    latent = mine[:, qw:]
    q_nope = query[:, :, :DN].astype(jnp.bfloat16)
    q_rope = rotate(query[:, :, DN:], theta[:, None, :]).astype(jnp.bfloat16)
    c_new = rms_scale(latent[:, :KVL], kv_gain).astype(jnp.bfloat16)
    k_rope = rotate(latent[:, KVL:], theta).astype(jnp.bfloat16)
    pack = jnp.concatenate(
        [q_nope.reshape(own, H * DN), q_rope.reshape(own, H * DR), c_new, k_rope], axis=1
    )
    every_pack = gather_rows(pack, "seq", n)
    q_nope_all = every_pack[:, : H * DN].reshape(tok_rows, H, DN)
    q_rope_all = every_pack[:, H * DN : H * (DN + DR)].reshape(tok_rows, H, DR)
    k_new_all = every_pack[:, H * (DN + DR) :]
    q_lat = jnp.einsum(
        "rhn,lhn->rhl", q_nope_all, expand[:, :, 0, :], preferred_element_type=jnp.float32
    ).astype(jnp.bfloat16)
    q_cat = jnp.concatenate([q_lat, q_rope_all], axis=-1)
    q_rows = q_cat.reshape(head_rows, KVL + DR)

    row_len = jnp.repeat(lengths, NTOK * H)
    row_grp = jnp.repeat(groups, NTOK * H)
    span = cache.shape[1]
    places_here = me * span + jnp.arange(span, dtype=jnp.int32)
    live = places_here[None, :] < row_len[:, None]
    best = jnp.full((head_rows,), NEG, jnp.float32)
    mass = jnp.zeros((head_rows,), jnp.float32)
    acc = jnp.zeros((head_rows, KVL), jnp.float32)
    for group in range(cache.shape[0]):
        keys = cache[group]
        score = jnp.einsum("rc,jc->rj", q_rows, keys, preferred_element_type=jnp.float32) * scale
        hit = row_grp == group
        valid = live & hit[:, None]
        peak = jnp.max(jnp.where(valid, score, NEG), axis=1)
        expo = jnp.where(valid, jnp.exp(score - peak[:, None]), 0.0)
        summed = jnp.dot(
            expo.astype(jnp.bfloat16), keys[:, :KVL], preferred_element_type=jnp.float32
        )
        best = jnp.where(hit, peak, best)
        mass = jnp.where(hit, jnp.sum(expo, axis=1), mass)
        acc = jnp.where(hit[:, None], summed, acc)

    w_v = expand[:, :, 1, :]
    part_v = jnp.einsum(
        "thl,lhn->thn",
        acc.reshape(tok_rows, H, KVL),
        w_v.astype(jnp.float32),
        precision=lax.Precision.HIGHEST,
        preferred_element_type=jnp.float32,
    )
    out_rows = w_out.shape[0]
    per_head = DN // out_rows
    v_cols = part_v.reshape(tok_rows, n, out_rows).transpose(1, 0, 2)
    head_of = jnp.arange(n, dtype=jnp.int32) // per_head
    peak_to = best.reshape(tok_rows, H).T[head_of]
    mass_to = mass.reshape(tok_rows, H).T[head_of]
    send = jnp.concatenate([v_cols, peak_to[..., None], mass_to[..., None]], axis=-1)
    got = scatter_rows(send.reshape(n * tok_rows, out_rows + 2), "seq").reshape(
        n, tok_rows, out_rows + 2
    )
    peaks = got[:, :, out_rows]
    masses = got[:, :, out_rows + 1]
    my_head = me // per_head
    unit0 = (me % per_head) * out_rows
    q_head = lax.dynamic_index_in_dim(q_cat, my_head, 1, keepdims=False)
    fresh = jnp.dot(q_head, k_new_all.T, preferred_element_type=jnp.float32) * scale
    tok = jnp.arange(tok_rows, dtype=jnp.int32)
    causal = ((tok[None, :] // NTOK) == (tok[:, None] // NTOK)) & (tok[None, :] <= tok[:, None])
    fresh = jnp.where(causal, fresh, NEG)
    top = jnp.maximum(jnp.max(peaks, axis=0), jnp.max(fresh, axis=1))
    keep = jnp.exp(peaks - top[None, :])
    fresh_w = jnp.where(causal, jnp.exp(fresh - top[:, None]), 0.0)
    total_mass = jnp.sum(masses * keep, axis=0) + jnp.sum(fresh_w, axis=1)
    fresh_lat = jnp.dot(
        fresh_w.astype(jnp.bfloat16), k_new_all[:, :KVL], preferred_element_type=jnp.float32
    )
    w_v_mine = lax.dynamic_slice_in_dim(
        lax.dynamic_index_in_dim(w_v, my_head, 1, keepdims=False), unit0, out_rows, 1
    )
    fresh_v = jnp.dot(
        fresh_lat,
        w_v_mine.astype(jnp.float32),
        precision=lax.Precision.HIGHEST,
        preferred_element_type=jnp.float32,
    )
    total_v = jnp.sum(got[:, :, :out_rows] * keep[:, :, None], axis=0) + fresh_v
    value_cols = (total_v / total_mass[:, None]).astype(jnp.bfloat16)

    attn_part = jnp.dot(value_cols, w_out, preferred_element_type=jnp.float32)
    attn = sum_to_owner(attn_part, "seq", n)
    flat_own = lax.dynamic_slice_in_dim(flat, me * own, own, 0)
    resid_own = (flat_own.astype(jnp.float32) + attn).astype(jnp.bfloat16)
    normed2_own = rms_scale(resid_own, ffn_gain).astype(jnp.bfloat16)
    normed2_own, shared_full = lax.optimization_barrier((normed2_own, shared_full))
    everyone = ("rep", "seq")
    every = gather_rows(normed2_own, everyone, n * rep_count)
    all_rows = every.shape[0]
    gates = jax.nn.softmax(jnp.dot(every, w_router, preferred_element_type=jnp.float32), axis=-1)
    chosen = routes.reshape(all_rows, TOPK)
    local_exp = expert_in.shape[0]
    own_expert = me * local_exp
    match = chosen == own_expert
    used = jnp.any(match, axis=1)
    gate_col = lax.dynamic_index_in_dim(gates, own_expert, 1, keepdims=False)
    coef = jnp.where(used, gate_col, 0.0)
    cap = max(2, min(tok_rows, 2 * tok_rows * TOPK // (local_exp * n)))
    slots = rep_count * cap
    rank = jnp.cumsum(used.reshape(rep_count, tok_rows).astype(jnp.int32), axis=1) - 1
    slot_of = (jnp.arange(rep_count, dtype=jnp.int32)[:, None] * cap + rank).reshape(all_rows)
    slot_of = jnp.where(used, slot_of, -1)
    pick = jnp.arange(slots, dtype=jnp.int32)[:, None] == slot_of[None, :]
    gathered = jnp.dot(pick.astype(jnp.bfloat16), every, preferred_element_type=jnp.float32).astype(
        jnp.bfloat16
    )
    both = jnp.einsum("rd,kdf->krf", gathered, expert_in[0], preferred_element_type=jnp.float32)
    act = (jax.nn.silu(both[0]) * both[1]).astype(jnp.bfloat16)
    expert_y = jnp.dot(act, expert_out[0], preferred_element_type=jnp.float32)
    shared_both = jnp.einsum(
        "rd,kdf->krf", every, shared_full, preferred_element_type=jnp.float32
    )
    shared_act = (jax.nn.silu(shared_both[0]) * shared_both[1]).astype(jnp.bfloat16)
    shared_part = jnp.dot(shared_act, shared_out, preferred_element_type=jnp.float32)
    out_cols = shared_out.shape[1]
    pick_wide = pick.astype(jnp.float32)
    routed = lax.dot_general(
        pick_wide, expert_y, (((0,), (0,)), ((), ())), precision=lax.Precision.HIGHEST
    )
    routed = routed * coef[:, None]
    block = lax.dynamic_slice_in_dim(routed, me * out_cols, out_cols, 1) + shared_part
    dense = lax.dynamic_update_slice_in_dim(routed, block, me * out_cols, 1).astype(jnp.bfloat16)
    total = sum_to_owner(dense, everyone, n * rep_count)
    out_own = (resid_own.astype(jnp.float32) + total).astype(jnp.bfloat16)
    return gather_rows(out_own, "seq", n).reshape(tokens.shape)


def solution(mesh):
    placed = (
        P("rep", None, None),
        P("rep"),
        P("rep"),
        P(None, "seq", None),
        P(),
        P(),
        P("seq", None),
        P("seq", None),
        P("seq", None),
        P("seq", None),
        P(),
        P(),
        P(),
        P("seq", None, None, "rep"),
        P("seq", "rep", None),
        P(None, "seq", "rep"),
        P("rep", "seq"),
    )
    return jax.shard_map(
        per_device, mesh=mesh, in_specs=placed, out_specs=P("rep", None, None), check_vma=False
    )
```
